32 devices in a mesh: slab: 2 (over y), genome: 4 (over x, core), group: 4 (over z).
Axes of the slice: x: 2, y: 2, z: 4, core: 2. Of those that a mesh axis runs over, the one named last changes fastest.
Arguments:
- genotypes: bfloat16 [640, 12288], P(None, ('slab', 'genome', 'group')), parts along dimension 1, may hold values from -6 to 6
Outputs:
- ld_score: float32 [12288], P(('slab', 'genome', 'group')), parts along dimension 0
The draws below stay inside these ranges and needn't reach their ends.
There are 2 independent parts, one for each index of `slab`. The reference program is written for one: setup_inputs(seed, part) draws one part's arguments, and reference() takes and returns one part's arrays. A program takes and returns all parts, laid end to end along the dimension named above; each array names one. Nothing has to cross between parts.
All inputs are finite; a program needn't handle non-finite values.
Results may differ from the reference program's by a relative error of at most 0.0003.
Values may be sent and summed in bfloat16 or wider, within the bound.
No kernel may reach another device: no remote copies, remote signals or barrier semaphores. Data moves between devices by JAX's collectives and lax.ppermute only.
A program may use at most 64 MiB of HBM per device.

```python
import jax
import jax.numpy as jnp
from jax import lax

SAMP = 640
PANEL = 1536
VARIANTS = 6144
N_GENOME = 4


def block_scale(stream_key, extent, shards, smallest, largest):
    factor_of = 1.0
    for position, shards_of in shards:
        draws = jax.random.uniform(jax.random.fold_in(jax.random.fold_in(stream_key, 6), position), (shards_of,), jnp.float32, smallest / len(shards), largest / len(shards))
        factor_of = factor_of * jnp.repeat(jnp.exp(draws), extent[position] // shards_of).reshape((-1,) + (1,) * (len(extent) - 1 - position))
    return factor_of


def normal_values(own_key, dims, deviation, bound, pieces=(), kind=jnp.bfloat16):
    level = block_scale(own_key, dims, pieces, -0.22, 0.18) if pieces else 1.0
    drawn = jax.random.normal(own_key, dims, jnp.float32) * deviation * level
    return jnp.minimum(jnp.maximum(drawn, -bound), bound).astype(kind)


def setup_inputs(seed: int = 0, part: int = 0) -> dict:
    keys = jax.random.split(jax.random.key(seed), 2)
    part_splits = jax.random.split(jax.random.fold_in(keys[1], part), 2)
    genotypes = normal_values(part_splits[0], (SAMP, VARIANTS), 1.0, 6.0, ((1, 16),))
    return {"genotypes": genotypes}


def reference(genotypes):
    padded = jnp.pad(genotypes, ((0, 0), (0, PANEL)))
    scaling = 1.0 / SAMP

    def one_panel(which):
        begin = (which * PANEL).astype(jnp.int32)
        row_block = lax.dynamic_slice_in_dim(genotypes, begin, PANEL, 1)
        column_block = lax.dynamic_slice_in_dim(padded, begin, 2 * PANEL, 1)
        band = jnp.dot(row_block.T, column_block, preferred_element_type=jnp.float32) * scaling
        return jnp.sum(band * band, axis=1)

    scores = lax.map(one_panel, jnp.arange(N_GENOME, dtype=jnp.int32))
    return scores.reshape(VARIANTS)
```

```python
import jax
import jax.numpy as jnp
from jax import lax
from jax.sharding import PartitionSpec as P


def passed_along(block, axis, distance):
    devices = range(lax.axis_size(axis))
    route = [(i - distance, i) for i in devices if i - distance in devices]
    return lax.ppermute(block, axis, route)


def row_squares(rows, columns, scaling):
    band = (
        lax.dot_general(rows, columns, (((0,), (0,)), ((), ())), preferred_element_type=jnp.float32)
        * scaling
    )
    return jnp.sum(band * band, axis=1)


def general_plan(genotypes):
    scaling = 1.0 / genotypes.shape[0]
    gathered = lax.all_gather(genotypes, "group", axis=1, tiled=True)
    following = passed_along(gathered, "genome", -1)
    return row_squares(genotypes, gathered, scaling) + row_squares(genotypes, following, scaling)


def hub_plan(genotypes):
    scaling = 1.0 / genotypes.shape[0]
    own = genotypes
    adopt = lax.ppermute(own, "group", [(0, 1), (3, 2)])
    nbr = lax.ppermute(own, "group", [(1, 2), (2, 1)])
    far = lax.ppermute(adopt, "group", [(1, 2), (2, 1)])
    panel = [own, adopt, nbr, far]
    rows = [own, adopt]

    rows_next = [lax.ppermute(r, "genome", [(0, 0), (2, 2), (1, 3)]) for r in rows]
    panel_next = [lax.ppermute(c, "genome", [(1, 0), (3, 2), (2, 3)]) for c in panel]

    scores = []
    for r, rn in zip(rows, rows_next):
        within = sum(row_squares(r, c, scaling) for c in panel)
        following = sum(row_squares(rn, c, scaling) for c in panel_next)
        following = lax.ppermute(following, "genome", [(0, 0), (2, 2), (3, 1)])
        scores.append(within + following)

    at_hub = lax.ppermute(scores[0], "group", [(1, 1), (2, 2)])
    at_end = lax.ppermute(scores[1], "group", [(1, 0), (2, 3)])
    return at_hub + at_end


def solution(mesh):
    placed = (P(None, ("slab", "genome", "group")),)
    hub = mesh.shape["group"] == 4 and mesh.shape["genome"] == 4
    return jax.shard_map(
        hub_plan if hub else general_plan,
        mesh=mesh,
        in_specs=placed,
        out_specs=P(("slab", "genome", "group")),
        check_vma=False,
    )
```

```python
import jax
import jax.numpy as jnp
from jax import lax
from jax.sharding import PartitionSpec as P


def passed_along(block, axis, distance):
    devices = range(lax.axis_size(axis))
    route = [(i - distance, i) for i in devices if i - distance in devices]
    return lax.ppermute(block, axis, route)


def row_squares(rows, columns, scaling):
    band = (
        lax.dot_general(rows, columns, (((0,), (0,)), ((), ())), preferred_element_type=jnp.float32)
        * scaling
    )
    return jnp.sum(band * band, axis=1)


def general_plan(genotypes):
    scaling = 1.0 / genotypes.shape[0]
    gathered = lax.all_gather(genotypes, "group", axis=1, tiled=True)
    following = passed_along(gathered, "genome", -1)
    return row_squares(genotypes, gathered, scaling) + row_squares(genotypes, following, scaling)


def hub_plan(genotypes):
    scaling = 1.0 / genotypes.shape[0]
    own = genotypes
    adopt = lax.ppermute(own, "group", [(0, 1), (3, 2)])
    nbr = lax.ppermute(own, "group", [(1, 2), (2, 1)])
    far = lax.ppermute(adopt, "group", [(1, 2), (2, 1)])
    panel = [own, adopt, nbr, far]

    onward = [(g, g + 1) for g in range(lax.axis_size("genome") - 1)]
    backward = [(b, a) for a, b in onward]
    rows = [own, adopt] + [lax.ppermute(r, "genome", onward) for r in (own, adopt)]
    sums = [sum(row_squares(r, c, scaling) for c in panel) for r in rows]
    following = lax.ppermute(jnp.concatenate(sums[2:]), "genome", backward)
    width = own.shape[1]
    at_hub = sums[0] + following[:width]
    adopted = sums[1] + following[width:]
    at_end = lax.ppermute(adopted, "group", [(1, 0), (2, 3)])
    place = lax.axis_index("group")
    return jnp.where((place == 1) | (place == 2), at_hub, at_end)


def solution(mesh):
    placed = (P(None, ("slab", "genome", "group")),)
    hub = mesh.shape["group"] == 4 and mesh.shape["genome"] == 4
    return jax.shard_map(
        hub_plan if hub else general_plan,
        mesh=mesh,
        in_specs=placed,
        out_specs=P(("slab", "genome", "group")),
        check_vma=False,
    )
```

```python
import jax
import jax.numpy as jnp
from jax import lax
from jax.sharding import PartitionSpec as P


def passed_along(block, axis, distance):
    devices = range(lax.axis_size(axis))
    route = [(i - distance, i) for i in devices if i - distance in devices]
    return lax.ppermute(block, axis, route)


def row_squares(rows, columns, scaling):
    band = (
        lax.dot_general(rows, columns, (((0,), (0,)), ((), ())), preferred_element_type=jnp.float32)
        * scaling
    )
    return jnp.sum(band * band, axis=1)


def general_plan(genotypes):
    scaling = 1.0 / genotypes.shape[0]
    gathered = lax.all_gather(genotypes, "group", axis=1, tiled=True)
    following = passed_along(gathered, "genome", -1)
    return row_squares(genotypes, gathered, scaling) + row_squares(genotypes, following, scaling)


def hub_plan(genotypes):
    scaling = 1.0 / genotypes.shape[0]
    own = genotypes
    adopt = lax.ppermute(own, "group", [(0, 1), (3, 2)])
    nbr = lax.ppermute(own, "group", [(1, 2), (2, 1)])
    far = lax.ppermute(adopt, "group", [(1, 2), (2, 1)])
    panel = [own, adopt, nbr, far]

    onward = [(g, g + 1) for g in range(lax.axis_size("genome") - 1)]
    backward = [(b, a) for a, b in onward]
    prev_own = lax.ppermute(own, "genome", onward)
    relay, _ = lax.optimization_barrier((prev_own, adopt))
    prev_adopt = lax.ppermute(relay, "group", [(0, 1), (3, 2)])
    rows = [own, adopt, prev_own, prev_adopt]
    sums = [sum(row_squares(r, c, scaling) for c in panel) for r in rows]
    following = lax.ppermute(jnp.concatenate(sums[2:]), "genome", backward)
    width = own.shape[1]
    at_hub = sums[0] + following[:width]
    adopted = sums[1] + following[width:]
    at_end = lax.ppermute(adopted, "group", [(1, 0), (2, 3)])
    place = lax.axis_index("group")
    return jnp.where((place == 1) | (place == 2), at_hub, at_end)


def solution(mesh):
    placed = (P(None, ("slab", "genome", "group")),)
    hub = mesh.shape["group"] == 4 and mesh.shape["genome"] == 4
    return jax.shard_map(
        hub_plan if hub else general_plan,
        mesh=mesh,
        in_specs=placed,
        out_specs=P(("slab", "genome", "group")),
        check_vma=False,
    )
```

```python
import jax
import jax.numpy as jnp
from jax import lax
from jax.sharding import PartitionSpec as P


def passed_along(block, axis, distance):
    devices = range(lax.axis_size(axis))
    route = [(i - distance, i) for i in devices if i - distance in devices]
    return lax.ppermute(block, axis, route)


def row_squares(rows, columns, scaling):
    band = (
        lax.dot_general(rows, columns, (((0,), (0,)), ((), ())), preferred_element_type=jnp.float32)
        * scaling
    )
    return jnp.sum(band * band, axis=1)


def general_plan(genotypes):
    scaling = 1.0 / genotypes.shape[0]
    gathered = lax.all_gather(genotypes, "group", axis=1, tiled=True)
    following = passed_along(gathered, "genome", -1)
    return row_squares(genotypes, gathered, scaling) + row_squares(genotypes, following, scaling)


def hub_plan(genotypes):
    scaling = 1.0 / genotypes.shape[0]
    own = genotypes
    adopt = lax.ppermute(own, "group", [(0, 1), (3, 2)])
    nbr = lax.ppermute(own, "group", [(1, 2), (2, 1)])
    far = lax.ppermute(adopt, "group", [(1, 2), (2, 1)])
    early = jnp.concatenate([own, adopt, nbr], axis=1)

    onward = [(g, g + 1) for g in range(lax.axis_size("genome") - 1)]
    backward = [(b, a) for a, b in onward]
    prev = [lax.ppermute(r, "genome", onward) for r in (own, adopt)]
    width = own.shape[1]
    sums = []
    for rows in (jnp.concatenate([own, adopt], axis=1), jnp.concatenate(prev, axis=1)):
        total = row_squares(rows, early, scaling) + row_squares(rows, far, scaling)
        sums += [total[:width], total[width:]]
    following = lax.ppermute(jnp.concatenate(sums[2:]), "genome", backward)
    at_hub = sums[0] + following[:width]
    adopted = sums[1] + following[width:]
    at_end = lax.ppermute(adopted, "group", [(1, 0), (2, 3)])
    place = lax.axis_index("group")
    return jnp.where((place == 1) | (place == 2), at_hub, at_end)


def solution(mesh):
    placed = (P(None, ("slab", "genome", "group")),)
    hub = mesh.shape["group"] == 4 and mesh.shape["genome"] == 4
    return jax.shard_map(
        hub_plan if hub else general_plan,
        mesh=mesh,
        in_specs=placed,
        out_specs=P(("slab", "genome", "group")),
        check_vma=False,
    )
```

```python
import jax
import jax.numpy as jnp
from jax import lax
from jax.sharding import PartitionSpec as P


def passed_along(block, axis, distance):
    devices = range(lax.axis_size(axis))
    route = [(i - distance, i) for i in devices if i - distance in devices]
    return lax.ppermute(block, axis, route)


def row_squares(rows, columns, scaling):
    band = (
        lax.dot_general(rows, columns, (((0,), (0,)), ((), ())), preferred_element_type=jnp.float32)
        * scaling
    )
    return jnp.sum(band * band, axis=1)


def general_plan(genotypes):
    scaling = 1.0 / genotypes.shape[0]
    gathered = lax.all_gather(genotypes, "group", axis=1, tiled=True)
    following = passed_along(gathered, "genome", -1)
    return row_squares(genotypes, gathered, scaling) + row_squares(genotypes, following, scaling)


def hub_plan(genotypes):
    scaling = 1.0 / genotypes.shape[0]
    own = genotypes
    adopt = lax.ppermute(own, "group", [(0, 1), (3, 2)])
    nbr = lax.ppermute(own, "group", [(1, 2), (2, 1)])
    far = lax.ppermute(adopt, "group", [(1, 2), (2, 1)])
    early = jnp.concatenate([own, adopt, nbr], axis=1)

    onward = [(g, g + 1) for g in range(lax.axis_size("genome") - 1)]
    backward = [(b, a) for a, b in onward]
    prev_own = lax.ppermute(own, "genome", onward)
    relay, _ = lax.optimization_barrier((prev_own, adopt))
    prev_adopt = lax.ppermute(relay, "group", [(0, 1), (3, 2)])
    width = own.shape[1]
    pair = jnp.concatenate([own, adopt], axis=1)
    total = row_squares(pair, early, scaling) + row_squares(pair, far, scaling)
    sums = [total[:width], total[width:]]
    for rows in (prev_own, prev_adopt):
        sums.append(row_squares(rows, early, scaling) + row_squares(rows, far, scaling))
    following = lax.ppermute(jnp.concatenate(sums[2:]), "genome", backward)
    at_hub = sums[0] + following[:width]
    adopted = sums[1] + following[width:]
    at_end = lax.ppermute(adopted, "group", [(1, 0), (2, 3)])
    place = lax.axis_index("group")
    return jnp.where((place == 1) | (place == 2), at_hub, at_end)


def solution(mesh):
    placed = (P(None, ("slab", "genome", "group")),)
    hub = mesh.shape["group"] == 4 and mesh.shape["genome"] == 4
    return jax.shard_map(
        hub_plan if hub else general_plan,
        mesh=mesh,
        in_specs=placed,
        out_specs=P(("slab", "genome", "group")),
        check_vma=False,
    )
```

```python
import jax
import jax.numpy as jnp
from jax import lax
from jax.sharding import PartitionSpec as P


def passed_along(block, axis, distance):
    devices = range(lax.axis_size(axis))
    route = [(i - distance, i) for i in devices if i - distance in devices]
    return lax.ppermute(block, axis, route)


def row_squares(rows, columns, scaling):
    band = (
        lax.dot_general(rows, columns, (((0,), (0,)), ((), ())), preferred_element_type=jnp.float32)
        * scaling
    )
    return jnp.sum(band * band, axis=1)


def general_plan(genotypes):
    scaling = 1.0 / genotypes.shape[0]
    gathered = lax.all_gather(genotypes, "group", axis=1, tiled=True)
    following = passed_along(gathered, "genome", -1)
    return row_squares(genotypes, gathered, scaling) + row_squares(genotypes, following, scaling)


def hub_plan(genotypes):
    scaling = 1.0 / genotypes.shape[0]
    own = genotypes
    adopt = lax.ppermute(own, "group", [(0, 1), (3, 2)])
    nbr = lax.ppermute(own, "group", [(1, 2), (2, 1)])
    far = lax.ppermute(adopt, "group", [(1, 2), (2, 1)])
    early = jnp.concatenate([own, adopt, nbr], axis=1)

    onward = [(g, g + 1) for g in range(lax.axis_size("genome") - 1)]
    backward = [(b, a) for a, b in onward]
    prev_own, prev_adopt = [lax.ppermute(r, "genome", onward) for r in (own, adopt)]
    width = own.shape[1]
    held = jnp.concatenate([own, adopt, prev_own], axis=1)
    total = row_squares(held, early, scaling) + row_squares(held, far, scaling)
    sums = [total[:width], total[width:2 * width], total[2 * width:]]
    sums.append(row_squares(prev_adopt, early, scaling) + row_squares(prev_adopt, far, scaling))
    following = lax.ppermute(jnp.concatenate(sums[2:]), "genome", backward)
    at_hub = sums[0] + following[:width]
    adopted = sums[1] + following[width:]
    at_end = lax.ppermute(adopted, "group", [(1, 0), (2, 3)])
    place = lax.axis_index("group")
    return jnp.where((place == 1) | (place == 2), at_hub, at_end)


def solution(mesh):
    placed = (P(None, ("slab", "genome", "group")),)
    hub = mesh.shape["group"] == 4 and mesh.shape["genome"] == 4
    return jax.shard_map(
        hub_plan if hub else general_plan,
        mesh=mesh,
        in_specs=placed,
        out_specs=P(("slab", "genome", "group")),
        check_vma=False,
    )
```

```python
import jax
import jax.numpy as jnp
from jax import lax
from jax.sharding import PartitionSpec as P


def passed_along(block, axis, distance):
    devices = range(lax.axis_size(axis))
    route = [(i - distance, i) for i in devices if i - distance in devices]
    return lax.ppermute(block, axis, route)


def row_squares(rows, columns, scaling):
    band = (
        lax.dot_general(rows, columns, (((0,), (0,)), ((), ())), preferred_element_type=jnp.float32)
        * scaling
    )
    return jnp.sum(band * band, axis=1)


def general_plan(genotypes):
    scaling = 1.0 / genotypes.shape[0]
    gathered = lax.all_gather(genotypes, "group", axis=1, tiled=True)
    following = passed_along(gathered, "genome", -1)
    return row_squares(genotypes, gathered, scaling) + row_squares(genotypes, following, scaling)


def hub_plan(genotypes):
    scaling = 1.0 / genotypes.shape[0]
    own = genotypes
    cut = min(256, own.shape[1])
    pieces = [own[:, :cut], own[:, cut:]] if cut < own.shape[1] else [own]
    adopt_parts = [lax.ppermute(p, "group", [(0, 1), (3, 2)]) for p in pieces]
    nbr = lax.ppermute(own, "group", [(1, 2), (2, 1)])
    far_parts = [lax.ppermute(p, "group", [(1, 2), (2, 1)]) for p in adopt_parts]
    adopt = jnp.concatenate(adopt_parts, axis=1) if len(adopt_parts) > 1 else adopt_parts[0]
    far = jnp.concatenate(far_parts, axis=1) if len(far_parts) > 1 else far_parts[0]
    early = jnp.concatenate([own, adopt, nbr], axis=1)

    onward = [(g, g + 1) for g in range(lax.axis_size("genome") - 1)]
    backward = [(b, a) for a, b in onward]
    prev_own, prev_adopt = [lax.ppermute(r, "genome", onward) for r in (own, adopt)]
    width = own.shape[1]
    held = jnp.concatenate([own, adopt, prev_own], axis=1)
    total = row_squares(held, early, scaling) + row_squares(held, far, scaling)
    sums = [total[:width], total[width:2 * width], total[2 * width:]]
    sums.append(row_squares(prev_adopt, early, scaling) + row_squares(prev_adopt, far, scaling))
    following = lax.ppermute(jnp.concatenate(sums[2:]), "genome", backward)
    at_hub = sums[0] + following[:width]
    adopted = sums[1] + following[width:]
    at_end = lax.ppermute(adopted, "group", [(1, 0), (2, 3)])
    place = lax.axis_index("group")
    return jnp.where((place == 1) | (place == 2), at_hub, at_end)


def solution(mesh):
    placed = (P(None, ("slab", "genome", "group")),)
    hub = mesh.shape["group"] == 4 and mesh.shape["genome"] == 4
    return jax.shard_map(
        hub_plan if hub else general_plan,
        mesh=mesh,
        in_specs=placed,
        out_specs=P(("slab", "genome", "group")),
        check_vma=False,
    )
```

```python
import jax
import jax.numpy as jnp
from jax import lax
from jax.sharding import PartitionSpec as P


def passed_along(block, axis, distance):
    devices = range(lax.axis_size(axis))
    route = [(i - distance, i) for i in devices if i - distance in devices]
    return lax.ppermute(block, axis, route)


def row_squares(rows, columns, scaling):
    band = (
        lax.dot_general(rows, columns, (((0,), (0,)), ((), ())), preferred_element_type=jnp.float32)
        * scaling
    )
    return jnp.sum(band * band, axis=1)


def general_plan(genotypes):
    scaling = 1.0 / genotypes.shape[0]
    gathered = lax.all_gather(genotypes, "group", axis=1, tiled=True)
    following = passed_along(gathered, "genome", -1)
    return row_squares(genotypes, gathered, scaling) + row_squares(genotypes, following, scaling)


def hub_plan(genotypes):
    scaling = 1.0 / genotypes.shape[0]
    own = genotypes
    adopt = lax.ppermute(own, "group", [(0, 1), (3, 2)])
    nbr = lax.ppermute(own, "group", [(1, 2), (2, 1)])
    far = lax.ppermute(adopt, "group", [(1, 2), (2, 1)])
    early = jnp.concatenate([own, adopt, nbr], axis=1)

    both = ("genome", "group")
    line = lax.axis_size("group")
    onward = [(g * line + z, (g + 1) * line + z) for g in range(lax.axis_size("genome") - 1) for z in (1, 2)]
    backward = [(b, a) for a, b in onward]
    prev = [lax.ppermute(r, both, onward) for r in (own, adopt)]
    width = own.shape[1]
    sums = []
    for rows in (jnp.concatenate([own, adopt], axis=1), jnp.concatenate(prev, axis=1)):
        total = row_squares(rows, early, scaling) + row_squares(rows, far, scaling)
        sums += [total[:width], total[width:]]
    following = lax.ppermute(jnp.concatenate(sums[2:]), both, backward)
    at_hub = sums[0] + following[:width]
    adopted = sums[1] + following[width:]
    at_end = lax.ppermute(adopted, "group", [(1, 0), (2, 3)])
    place = lax.axis_index("group")
    return jnp.where((place == 1) | (place == 2), at_hub, at_end)


def solution(mesh):
    placed = (P(None, ("slab", "genome", "group")),)
    hub = mesh.shape["group"] == 4 and mesh.shape["genome"] == 4
    return jax.shard_map(
        hub_plan if hub else general_plan,
        mesh=mesh,
        in_specs=placed,
        out_specs=P(("slab", "genome", "group")),
        check_vma=False,
    )
```

```python
import jax
import jax.numpy as jnp
from jax import lax
from jax.sharding import PartitionSpec as P


def passed_along(block, axis, distance):
    devices = range(lax.axis_size(axis))
    route = [(i - distance, i) for i in devices if i - distance in devices]
    return lax.ppermute(block, axis, route)


def row_squares(rows, columns, scaling):
    band = (
        lax.dot_general(rows, columns, (((0,), (0,)), ((), ())), preferred_element_type=jnp.float32)
        * scaling
    )
    return jnp.sum(band * band, axis=1)


def general_plan(genotypes):
    scaling = 1.0 / genotypes.shape[0]
    gathered = lax.all_gather(genotypes, "group", axis=1, tiled=True)
    following = passed_along(gathered, "genome", -1)
    return row_squares(genotypes, gathered, scaling) + row_squares(genotypes, following, scaling)


def hub_plan(genotypes):
    scaling = 1.0 / genotypes.shape[0]
    own = genotypes
    adopt = lax.ppermute(own, "group", [(0, 1), (3, 2)])
    nbr = lax.ppermute(own, "group", [(1, 2), (2, 1)])

    both = ("genome", "group")
    line = lax.axis_size("group")
    steps = range(lax.axis_size("genome") - 1)
    crossing = [g for g in steps if g % 2 == 1]
    hubs = (1, 2)
    onward = [(g * line + z, (g + 1) * line + z) for g in steps for z in hubs]
    backward = [(b, a) for a, b in onward]
    ends_across = [(g * line + z, (g + 1) * line + z) for g in crossing for z in (0, line - 1)]
    prev_own = lax.ppermute(own, both, onward + ends_across)
    on_chip = [(g * line + z, (g + 1) * line + z) for g in steps if g % 2 == 0 for z in hubs]
    relay, adopted_here = lax.optimization_barrier((prev_own, adopt))
    far = lax.ppermute(adopted_here, "group", [(1, 2), (2, 1)])
    early = jnp.concatenate([own, adopt, nbr], axis=1)
    relayed = [((g + 1) * line, (g + 1) * line + 1) for g in crossing]
    relayed += [((g + 1) * line + line - 1, (g + 1) * line + line - 2) for g in crossing]
    prev_adopt = lax.ppermute(adopt, both, on_chip) + lax.ppermute(relay, both, relayed)
    prev = [prev_own, prev_adopt]
    width = own.shape[1]
    sums = []
    for rows in (jnp.concatenate([own, adopt], axis=1), jnp.concatenate(prev, axis=1)):
        total = row_squares(rows, early, scaling) + row_squares(rows, far, scaling)
        sums += [total[:width], total[width:]]
    following = lax.ppermute(jnp.concatenate(sums[2:]), both, backward)
    at_hub = sums[0] + following[:width]
    adopted = sums[1] + following[width:]
    at_end = lax.ppermute(adopted, "group", [(1, 0), (2, 3)])
    place = lax.axis_index("group")
    return jnp.where((place == 1) | (place == 2), at_hub, at_end)


def solution(mesh):
    placed = (P(None, ("slab", "genome", "group")),)
    hub = mesh.shape["group"] == 4 and mesh.shape["genome"] == 4
    return jax.shard_map(
        hub_plan if hub else general_plan,
        mesh=mesh,
        in_specs=placed,
        out_specs=P(("slab", "genome", "group")),
        check_vma=False,
    )
```

```python
import jax
import jax.numpy as jnp
from jax import lax
from jax.sharding import PartitionSpec as P


def passed_along(block, axis, distance):
    devices = range(lax.axis_size(axis))
    route = [(i - distance, i) for i in devices if i - distance in devices]
    return lax.ppermute(block, axis, route)


def row_squares(rows, columns, scaling):
    band = (
        lax.dot_general(rows, columns, (((0,), (0,)), ((), ())), preferred_element_type=jnp.float32)
        * scaling
    )
    return jnp.sum(band * band, axis=1)


def general_plan(genotypes):
    scaling = 1.0 / genotypes.shape[0]
    gathered = lax.all_gather(genotypes, "group", axis=1, tiled=True)
    following = passed_along(gathered, "genome", -1)
    return row_squares(genotypes, gathered, scaling) + row_squares(genotypes, following, scaling)


def hub_plan(genotypes):
    scaling = 1.0 / genotypes.shape[0]
    own = genotypes
    adopt = lax.ppermute(own, "group", [(0, 1), (3, 2)])
    nbr = lax.ppermute(own, "group", [(1, 2), (2, 1)])

    both = ("genome", "group")
    line = lax.axis_size("group")
    steps = range(lax.axis_size("genome") - 1)
    crossing = [g for g in steps if g % 2 == 1]
    hubs = (1, 2)
    onward = [(g * line + z, (g + 1) * line + z) for g in steps for z in hubs]
    backward = [(b, a) for a, b in onward]
    ends_across = [(g * line + z, (g + 1) * line + z) for g in crossing for z in (0, line - 1)]
    prev_own = lax.ppermute(own, both, onward + ends_across)
    on_chip = [(g * line + z, (g + 1) * line + z) for g in steps if g % 2 == 0 for z in hubs]
    relay, adopted_here = lax.optimization_barrier((prev_own, adopt))
    far = lax.ppermute(adopted_here, "group", [(1, 2), (2, 1)])
    early = jnp.concatenate([own, adopt, nbr], axis=1)
    relayed = [((g + 1) * line, (g + 1) * line + 1) for g in crossing]
    relayed += [((g + 1) * line + line - 1, (g + 1) * line + line - 2) for g in crossing]
    prev_adopt = lax.ppermute(adopt, both, on_chip) + lax.ppermute(relay, both, relayed)
    prev = [prev_own, prev_adopt]
    width = own.shape[1]
    sums = []
    for rows in (jnp.concatenate([own, adopt], axis=1), jnp.concatenate(prev, axis=1)):
        total = row_squares(rows, early, scaling) + row_squares(rows, far, scaling)
        sums += [total[:width], total[width:]]
    returned = jnp.concatenate(sums[2:])
    back_within = [(a, b) for a, b in backward if (b // line) % 2 == 0]
    back_across = [(a, b) for a, b in backward if (b // line) % 2 == 1]
    following = lax.ppermute(returned, both, back_within) + lax.ppermute(returned, both, back_across)
    at_hub = sums[0] + following[:width]
    adopted = sums[1] + following[width:]
    at_end = lax.ppermute(adopted, "group", [(1, 0), (2, 3)])
    place = lax.axis_index("group")
    return jnp.where((place == 1) | (place == 2), at_hub, at_end)


def solution(mesh):
    placed = (P(None, ("slab", "genome", "group")),)
    hub = mesh.shape["group"] == 4 and mesh.shape["genome"] == 4
    return jax.shard_map(
        hub_plan if hub else general_plan,
        mesh=mesh,
        in_specs=placed,
        out_specs=P(("slab", "genome", "group")),
        check_vma=False,
    )
```

```python
import jax
import jax.numpy as jnp
from jax import lax
from jax.sharding import PartitionSpec as P


def passed_along(block, axis, distance):
    devices = range(lax.axis_size(axis))
    route = [(i - distance, i) for i in devices if i - distance in devices]
    return lax.ppermute(block, axis, route)


def row_squares(rows, columns, scaling):
    band = (
        lax.dot_general(rows, columns, (((0,), (0,)), ((), ())), preferred_element_type=jnp.float32)
        * scaling
    )
    return jnp.sum(band * band, axis=1)


def general_plan(genotypes):
    scaling = 1.0 / genotypes.shape[0]
    gathered = lax.all_gather(genotypes, "group", axis=1, tiled=True)
    following = passed_along(gathered, "genome", -1)
    return row_squares(genotypes, gathered, scaling) + row_squares(genotypes, following, scaling)


def hub_plan(genotypes):
    scaling = 1.0 / genotypes.shape[0]
    own = genotypes
    adopt = lax.ppermute(own, "group", [(0, 1), (3, 2)])
    nbr = lax.ppermute(own, "group", [(1, 2), (2, 1)])

    both = ("genome", "group")
    line = lax.axis_size("group")
    steps = range(lax.axis_size("genome") - 1)
    crossing = [g for g in steps if g % 2 == 1]
    hubs = (1, 2)
    onward = [(g * line + z, (g + 1) * line + z) for g in steps for z in hubs]
    backward = [(b, a) for a, b in onward]
    ends_across = [(g * line + z, (g + 1) * line + z) for g in crossing for z in (0, line - 1)]
    prev_own = lax.ppermute(own, both, onward + ends_across)
    on_chip = [(g * line + z, (g + 1) * line + z) for g in steps if g % 2 == 0 for z in hubs]
    relay, adopted_here = lax.optimization_barrier((prev_own, adopt))
    far = lax.ppermute(adopted_here, "group", [(1, 2), (2, 1)])
    early = jnp.concatenate([own, adopt, nbr], axis=1)
    relayed = [((g + 1) * line, (g + 1) * line + 1) for g in crossing]
    relayed += [((g + 1) * line + line - 1, (g + 1) * line + line - 2) for g in crossing]
    prev_adopt = lax.ppermute(adopt, both, on_chip) + lax.ppermute(relay, both, relayed)
    prev = [prev_own, prev_adopt]
    width = own.shape[1]
    sums = []
    for rows in (jnp.concatenate([own, adopt], axis=1), jnp.concatenate(prev, axis=1)):
        total = row_squares(rows, early, scaling) + row_squares(rows, far, scaling)
        sums += [total[:width], total[width:]]
    to_end = [((g + 1) * line + 1, g * line) for g in steps]
    to_end += [((g + 1) * line + line - 2, g * line + line - 1) for g in steps]
    at_hub = sums[0] + lax.ppermute(sums[2], both, backward)
    at_end = lax.ppermute(sums[1], "group", [(1, 0), (2, 3)]) + lax.ppermute(sums[3], both, to_end)
    place = lax.axis_index("group")
    return jnp.where((place == 1) | (place == 2), at_hub, at_end)


def solution(mesh):
    placed = (P(None, ("slab", "genome", "group")),)
    hub = mesh.shape["group"] == 4 and mesh.shape["genome"] == 4
    return jax.shard_map(
        hub_plan if hub else general_plan,
        mesh=mesh,
        in_specs=placed,
        out_specs=P(("slab", "genome", "group")),
        check_vma=False,
    )
```

```python
import jax
import jax.numpy as jnp
from jax import lax
from jax.sharding import PartitionSpec as P


def passed_along(block, axis, distance):
    devices = range(lax.axis_size(axis))
    route = [(i - distance, i) for i in devices if i - distance in devices]
    return lax.ppermute(block, axis, route)


def row_squares(rows, columns, scaling):
    band = (
        lax.dot_general(rows, columns, (((0,), (0,)), ((), ())), preferred_element_type=jnp.float32)
        * scaling
    )
    return jnp.sum(band * band, axis=1)


def general_plan(genotypes):
    scaling = 1.0 / genotypes.shape[0]
    gathered = lax.all_gather(genotypes, "group", axis=1, tiled=True)
    following = passed_along(gathered, "genome", -1)
    return row_squares(genotypes, gathered, scaling) + row_squares(genotypes, following, scaling)


def hub_plan(genotypes):
    scaling = 1.0 / genotypes.shape[0]
    own = genotypes
    adopt = lax.ppermute(own, "group", [(0, 1), (3, 2)])
    nbr = lax.ppermute(own, "group", [(1, 2), (2, 1)])

    both = ("genome", "group")
    line = lax.axis_size("group")
    steps = range(lax.axis_size("genome") - 1)
    crossing = [g for g in steps if g % 2 == 1]
    hubs = (1, 2)
    onward = [(g * line + z, (g + 1) * line + z) for g in steps for z in hubs]
    backward = [(b, a) for a, b in onward]
    ends_across = [(g * line + z, (g + 1) * line + z) for g in crossing for z in (0, line - 1)]
    prev_own = lax.ppermute(own, both, onward + ends_across)
    on_chip = [(g * line + z, (g + 1) * line + z) for g in steps if g % 2 == 0 for z in hubs]
    adopted_here, nbr = lax.optimization_barrier((adopt, nbr))
    relay, _ = lax.optimization_barrier((prev_own, adopted_here))
    far = lax.ppermute(adopted_here, "group", [(1, 2), (2, 1)])
    early = jnp.concatenate([own, adopt, nbr], axis=1)
    relayed = [((g + 1) * line, (g + 1) * line + 1) for g in crossing]
    relayed += [((g + 1) * line + line - 1, (g + 1) * line + line - 2) for g in crossing]
    prev_adopt = lax.ppermute(adopt, both, on_chip) + lax.ppermute(relay, both, relayed)
    prev = [prev_own, prev_adopt]
    width = own.shape[1]
    sums = []
    for rows in (jnp.concatenate([own, adopt], axis=1), jnp.concatenate(prev, axis=1)):
        total = row_squares(rows, early, scaling) + row_squares(rows, far, scaling)
        sums += [total[:width], total[width:]]
    following = lax.ppermute(jnp.concatenate(sums[2:]), both, backward)
    at_hub = sums[0] + following[:width]
    adopted = sums[1] + following[width:]
    at_end = lax.ppermute(adopted, "group", [(1, 0), (2, 3)])
    place = lax.axis_index("group")
    return jnp.where((place == 1) | (place == 2), at_hub, at_end)


def solution(mesh):
    placed = (P(None, ("slab", "genome", "group")),)
    hub = mesh.shape["group"] == 4 and mesh.shape["genome"] == 4
    return jax.shard_map(
        hub_plan if hub else general_plan,
        mesh=mesh,
        in_specs=placed,
        out_specs=P(("slab", "genome", "group")),
        check_vma=False,
    )
```

```python
import jax
import jax.numpy as jnp
from jax import lax
from jax.sharding import PartitionSpec as P


def passed_along(block, axis, distance):
    devices = range(lax.axis_size(axis))
    route = [(i - distance, i) for i in devices if i - distance in devices]
    return lax.ppermute(block, axis, route)


def row_squares(rows, columns, scaling):
    band = (
        lax.dot_general(rows, columns, (((0,), (0,)), ((), ())), preferred_element_type=jnp.float32)
        * scaling
    )
    return jnp.sum(band * band, axis=1)


def general_plan(genotypes):
    scaling = 1.0 / genotypes.shape[0]
    gathered = lax.all_gather(genotypes, "group", axis=1, tiled=True)
    following = passed_along(gathered, "genome", -1)
    return row_squares(genotypes, gathered, scaling) + row_squares(genotypes, following, scaling)


def hub_plan(genotypes):
    scaling = 1.0 / genotypes.shape[0]
    own = genotypes
    adopt = lax.ppermute(own, "group", [(0, 1), (3, 2)])
    nbr = lax.ppermute(own, "group", [(1, 2), (2, 1)])

    both = ("genome", "group")
    line = lax.axis_size("group")
    steps = range(lax.axis_size("genome") - 1)
    crossing = [g for g in steps if g % 2 == 1]
    hubs = (1, 2)
    onward = [(g * line + z, (g + 1) * line + z) for g in steps for z in hubs]
    backward = [(b, a) for a, b in onward]
    ends_across = [(g * line + z, (g + 1) * line + z) for g in crossing for z in (0, line - 1)]
    prev_own = lax.ppermute(own, both, onward + ends_across)
    on_chip = [(g * line + z, (g + 1) * line + z) for g in steps if g % 2 == 0 for z in hubs]
    relay, adopted_here = lax.optimization_barrier((prev_own, adopt))
    far = lax.ppermute(adopted_here, "group", [(1, 2), (2, 1)])
    early = jnp.concatenate([own, adopt, nbr], axis=1)
    relayed = [((g + 1) * line, (g + 1) * line + 1) for g in crossing]
    relayed += [((g + 1) * line + line - 1, (g + 1) * line + line - 2) for g in crossing]
    prev_adopt = lax.ppermute(adopt, both, on_chip) + lax.ppermute(relay, both, relayed)
    prev = [prev_own, prev_adopt]
    width = own.shape[1]
    pair, prev_rows = jnp.concatenate([own, adopt], axis=1), jnp.concatenate(prev, axis=1)
    before = [row_squares(pair, early, scaling), row_squares(prev_rows, early, scaling)]
    far, before[1] = lax.optimization_barrier((far, before[1]))
    sums = []
    for rows, part in zip((pair, prev_rows), before):
        total = part + row_squares(rows, far, scaling)
        sums += [total[:width], total[width:]]
    to_end = [((g + 1) * line + 1, g * line) for g in steps]
    to_end += [((g + 1) * line + line - 2, g * line + line - 1) for g in steps]
    at_hub = sums[0] + lax.ppermute(sums[2], both, backward)
    at_end = lax.ppermute(sums[1], "group", [(1, 0), (2, 3)]) + lax.ppermute(sums[3], both, to_end)
    place = lax.axis_index("group")
    return jnp.where((place == 1) | (place == 2), at_hub, at_end)


def solution(mesh):
    placed = (P(None, ("slab", "genome", "group")),)
    hub = mesh.shape["group"] == 4 and mesh.shape["genome"] == 4
    return jax.shard_map(
        hub_plan if hub else general_plan,
        mesh=mesh,
        in_specs=placed,
        out_specs=P(("slab", "genome", "group")),
        check_vma=False,
    )
```
